256 devices in a mesh: section: 4 (over y), dp: 64 (over x, z, core).
Axes of the slice: x: 4, y: 4, z: 8, core: 2. Of those that a mesh axis runs over, the one named last changes fastest.
Arguments:
- grad_out: bfloat16 [12288, 1536], P('dp'), may hold values from -6 to 6
- section_inputs: bfloat16 [4, 12288, 1536], P('section', 'dp'), may hold values from -16 to 16
- lengths: int32 [256], replicated, may hold values from 1 to 48, 9216 in all
- bucket_list: int32 [256], P('dp'), may hold values from 0 to 255, each once
- conv_weight: float32 [4, 31, 1536], P('section'), may hold values from -8 to 8
- norm_gain: float32 [4, 1536], P('section'), may hold values from 0.5 to 1.5
- projection: bfloat16 [4, 1536, 1536], P('section'), may hold values from -0.15625 to 0.15625
Outputs:
- section_grads: bfloat16 [4, 12288, 1536], P('section', 'dp')
- projection_grad: float32 [4, 1536, 1536], P('section', 'dp')
- conv_grad: float32 [4, 31, 1536], P('section', None, 'dp')
- gain_grad: float32 [4, 1536], P('section', 'dp')
The draws below stay inside these ranges and needn't reach their ends.
All inputs are finite; a program needn't handle non-finite values.
Results may differ from the reference program's by a relative error of at most 0.0057.
Values may be sent and summed in bfloat16 or wider, within the bound.
No kernel may reach another device: no remote copies, remote signals or barrier semaphores. Data moves between devices by JAX's collectives and lax.ppermute only.
A program may use at most 128 MiB of HBM per device.

```python
import math
import jax
import jax.numpy as jnp
import numpy as np
from jax import lax

D = 1536
K = 31
P_SIZE = 48
M = 4
SECTIONS = 4
UTT_ALL = 256
TOKENS = 12288
N_DP = 64


def draw_conv_weight(key, part):
    first, second = jax.random.split(jax.random.fold_in(key, 17))
    base = jnp.clip(jax.random.normal(first, (SECTIONS, K, D), jnp.float32), -4.0, 4.0)
    spread = jnp.exp(jax.random.uniform(second, (SECTIONS, 1, D), jnp.float32, 0.0, math.log(10.0)))
    return base * spread / math.sqrt(K)


def strengthened(drawn, key, source, target, blocks, factor):
    def block_of(position):
        return (jnp.arange(drawn.shape[position]) // (drawn.shape[position] // blocks)).reshape((-1,) + (1,) * (drawn.ndim - 1 - position))

    first = jax.random.permutation(key, blocks)[block_of(target)]
    second = (block_of(target) + blocks // 2) % blocks
    return jnp.where((block_of(source) == first) | (block_of(source) == second), factor * drawn, drawn)


def block_levels(rng, extent, cuts, least, high):
    def one(axis_at, shards_of):
        heights = jax.random.uniform(jax.random.fold_in(jax.random.fold_in(rng, 6), axis_at), (shards_of,), jnp.float32, least / len(cuts), high / len(cuts))
        return jnp.repeat(jnp.exp(heights), extent[axis_at] // shards_of).reshape((-1,) + (1,) * (len(extent) - axis_at - 1))

    factor_of = one(*cuts[0])
    for cut in cuts[1:]:
        factor_of = factor_of * one(*cut)
    return factor_of


def length_profile(count, total, reach, lean):
    weights = [(1 << 20) // math.isqrt(grade ** lean) + 1 for grade in range(2, count + 1)]
    spare, given = total - reach - (count - 1), [1] * (count - 1)
    while spare > 0:
        free = [i for i in range(count - 1) if given[i] < reach]
        whole, budget = sum([weights[i] for i in free]), spare
        for i in free:
            addition = min(reach - given[i], max(1, budget * weights[i] // whole), spare)
            given[i] = given[i] + addition
            spare = spare - addition
    return np.array([reach] + given)


def uneven_parts(key, amount, total, most, slope):
    if amount == 2:
        one = jax.random.randint(key, (), max(1, total - most), min(most, total - 1) + 1)
        return jnp.stack([one, total - one])
    sizes = jnp.asarray(length_profile(amount, total, most, slope), jnp.int32)
    couples = (amount - 1) // 2
    giver, taker = sizes[1:1 + 2 * couples:2], sizes[2:2 + 2 * couples:2]
    margin = jnp.minimum(giver - 1, most - taker)
    passed = jax.random.randint(jax.random.fold_in(key, 1), (couples,), 0, 1 << 20) % (margin + 1)
    sizes = sizes.at[1:1 + 2 * couples:2].set(giver - passed).at[2:2 + 2 * couples:2].set(taker + passed)
    return sizes[jax.random.permutation(jax.random.fold_in(key, 2), amount)]


def bell_draw(key, extent, deviation, reach, pieces=(), kind=jnp.bfloat16):
    entries = jax.random.normal(key, extent, jnp.float32) * deviation
    if len(pieces) > 0:
        entries = block_levels(key, extent, pieces, -0.22, 0.18) * entries
    return jnp.clip(entries, min=-reach, max=reach).astype(kind)


def heavy_noise(rng, extent, width, reach, cuts, heavy, kind=jnp.bfloat16):
    result = width * jax.random.normal(rng, extent, jnp.float32)
    if cuts:
        result = result * block_levels(rng, extent, cuts, -0.22, 0.18)
    return jnp.clip(strengthened(result, jax.random.fold_in(rng, 3), *heavy), -reach, reach).astype(kind)


def setup_inputs(seed: int = 0) -> dict:
    keys = jax.random.split(jax.random.key(seed), 8)
    grad_out = bell_draw(keys[0], (TOKENS, D), 1.0, 6.0, ((0, 64),))
    section_inputs = heavy_noise(keys[1], (SECTIONS, TOKENS, D), 1.0, 16.0, ((0, 4), (1, 64)), (1, 2, 64, 4.0))
    lengths = uneven_parts(keys[2], UTT_ALL, UTT_ALL * P_SIZE * 3 // 4, P_SIZE, 1).astype(jnp.int32)
    bucket_list = jax.random.permutation(keys[3], UTT_ALL).astype(jnp.int32)
    conv_weight = draw_conv_weight(jax.random.fold_in(keys[7], 71), 0)
    norm_gain = jnp.clip(1.0 + 0.1 * jax.random.normal(keys[5], (SECTIONS, D), jnp.float32), 0.5, 1.5)
    projection = bell_draw(keys[6], (SECTIONS, D, D), D ** -0.5, 0.15625, ((0, 4),))
    return {"grad_out": grad_out, "section_inputs": section_inputs, "lengths": lengths, "bucket_list": bucket_list, "conv_weight": conv_weight, "norm_gain": norm_gain, "projection": projection}


eps = 1e-05

def layer_backward(x, dy, mask, kernel, gain, proj):
    half = (kernel.shape[0] - 1) // 2
    frames = x.shape[1]
    u = x.astype(jnp.float32) * mask
    upad = jnp.pad(u, ((0, 0), (half, half), (0, 0)))
    a = jnp.zeros(u.shape, jnp.float32)
    for j in range(kernel.shape[0]):
        a = a + kernel[j] * upad[:, j:j + frames]
    mean = lax.optimization_barrier(jnp.mean(a, axis=-1, keepdims=True))
    cen = a - mean
    var = lax.optimization_barrier(jnp.mean(cen * cen, axis=-1, keepdims=True))
    inv = lax.rsqrt(var + eps)
    nhat = cen * inv
    n = nhat * gain
    sig = jax.nn.sigmoid(n)
    h = (n * sig).astype(jnp.bfloat16)
    dz = (dy.astype(jnp.float32) * mask).astype(jnp.bfloat16)
    dh = jnp.einsum('upe,de->upd', dz.astype(jnp.float32), proj.astype(jnp.float32))
    dn = dh * (sig + n * sig * (1.0 - sig))
    dgain = lax.optimization_barrier(jnp.sum(dn * nhat, axis=(0, 1)))
    dnh = dn * gain
    da = inv * (dnh - lax.optimization_barrier(jnp.mean(dnh, axis=-1, keepdims=True)) - nhat * lax.optimization_barrier(jnp.mean(dnh * nhat, axis=-1, keepdims=True)))
    dapad = jnp.pad(da, ((0, 0), (half, half), (0, 0)))
    du = jnp.zeros(u.shape, jnp.float32)
    for j in range(kernel.shape[0]):
        du = du + kernel[j] * dapad[:, 2 * half - j:2 * half - j + frames]
    dconv = jnp.stack([lax.optimization_barrier(jnp.sum(da * upad[:, j:j + frames], axis=(0, 1))) for j in range(kernel.shape[0])])
    dx = (dy.astype(jnp.float32) + mask * du).astype(jnp.bfloat16)
    return (dx, h, dz, dgain, dconv)

def reference(grad_out, section_inputs, lengths, bucket_list, conv_weight, norm_gain, projection):
    lens = jnp.take(lengths, bucket_list)
    block = M * P_SIZE

    def group(carry, index):
        proj_acc, conv_acc, gain_acc = carry
        dy = lax.dynamic_slice_in_dim(grad_out, index * block, block, 0).reshape(M, P_SIZE, D)
        saved = lax.dynamic_slice_in_dim(section_inputs, index * block, block, 1).reshape(SECTIONS, M, P_SIZE, D)
        local_lens = lax.dynamic_slice_in_dim(lens, index * M, M, 0)
        mask = (jnp.arange(P_SIZE, dtype=jnp.int32)[None, :] < local_lens[:, None]).astype(jnp.float32)[..., None]
        results = [None] * SECTIONS
        for s in reversed(range(SECTIONS)):
            dx, h, dz, dgain, dconv = layer_backward(saved[s], dy, mask, conv_weight[s], norm_gain[s], projection[s])
            term = jnp.dot(h.reshape(block, D).T, dz.reshape(block, D), preferred_element_type=jnp.float32)
            proj_acc = proj_acc.at[s].add(term)
            conv_acc = conv_acc.at[s].add(dconv)
            gain_acc = gain_acc.at[s].add(dgain)
            results[s] = dx.reshape(block, D)
            dy = dx
        return ((proj_acc, conv_acc, gain_acc), jnp.stack(results))
    init = (jnp.zeros((SECTIONS, D, D), jnp.float32), jnp.zeros((SECTIONS, K, D), jnp.float32), jnp.zeros((SECTIONS, D), jnp.float32))
    (proj_acc, conv_acc, gain_acc), outs = lax.scan(group, init, jnp.arange(N_DP, dtype=jnp.int32))
    section_grads = jnp.transpose(outs, (1, 0, 2, 3)).reshape(SECTIONS, TOKENS, D)
    scale = 1.0 / N_DP
    return (section_grads, proj_acc * scale, conv_acc * scale, gain_acc * scale)
```

```python
import jax
import jax.numpy as jnp
from jax import lax
from jax.sharding import PartitionSpec as P

eps = 1e-05


def from_behind(value, axis, by):
    size = lax.axis_size(axis)
    pairs = [(i, i + by) for i in range(size) if 0 <= i + by < size]
    return lax.ppermute(value, axis, pairs)


def layer_forward(x, mask, kernel):
    taps = kernel.shape[0]
    half = (taps - 1) // 2
    frames = x.shape[1]
    u = x.astype(jnp.float32) * mask
    upad = jnp.pad(u, ((0, 0), (half, half), (0, 0)))
    a = jnp.zeros(u.shape, jnp.float32)
    for j in range(taps):
        a = a + kernel[j] * upad[:, j : j + frames]
    return upad, a


def norm_forward(a, gain):
    mean = jnp.mean(a, axis=-1, keepdims=True)
    cen = a - mean
    var = jnp.mean(cen * cen, axis=-1, keepdims=True)
    inv = lax.rsqrt(var + eps)
    nhat = cen * inv
    n = nhat * gain
    sig = jax.nn.sigmoid(n)
    h = (n * sig).astype(jnp.bfloat16)
    slope = sig + n * sig * (1.0 - sig)
    return inv, nhat, h, slope


def layer_backward(dy, mask, kernel, gain, proj, inv, nhat, slope):
    taps = kernel.shape[0]
    half = (taps - 1) // 2
    frames = dy.shape[0]
    dz = (dy.astype(jnp.float32) * mask).astype(jnp.bfloat16)
    dh = lax.dot_general(dz, proj, (((1,), (1,)), ((), ())), preferred_element_type=jnp.float32)
    dn = dh * slope
    dnh = dn * gain
    da = inv * (
        dnh
        - jnp.mean(dnh, axis=-1, keepdims=True)
        - nhat * jnp.mean(dnh * nhat, axis=-1, keepdims=True)
    )
    dapad = jnp.pad(da, ((half, half), (0, 0)))
    du = jnp.zeros(da.shape, jnp.float32)
    for j in range(taps):
        du = du + kernel[j] * dapad[2 * half - j : 2 * half - j + frames]
    dx = (dy.astype(jnp.float32) + mask * du).astype(jnp.bfloat16)
    return dx, dz, dn, da


def body(grad_out, section_inputs, lengths, bucket_list, conv_weight, norm_gain, projection):
    sections = lax.axis_size("section")
    groups = lax.axis_size("dp")
    rank = lax.axis_index("section")
    micro = bucket_list.shape[0]
    rows, width = grad_out.shape
    frames = rows // micro
    table = jnp.arange(lengths.shape[0], dtype=jnp.int32)
    lens = jnp.sum(jnp.where(bucket_list[:, None] == table[None, :], lengths[None, :], 0), axis=1)
    masks = (jnp.arange(frames, dtype=jnp.int32)[None, :] < lens[:, None]).astype(jnp.float32)[
        ..., None
    ]
    saved = section_inputs[0].reshape(micro, frames, width)
    top = grad_out.reshape(micro, frames, width)
    kernel = conv_weight[0]
    gain = norm_gain[0]
    proj = projection[0]
    taps = kernel.shape[0]

    upad, a = layer_forward(saved, masks, kernel)
    inv, nhat, h, slope = norm_forward(a, gain)

    dz_buf = jnp.zeros((micro, frames, width), jnp.bfloat16)
    dx_buf = jnp.zeros((micro, frames, width), jnp.bfloat16)
    dn_buf = jnp.zeros((micro, frames, width), jnp.float32)
    da_buf = jnp.zeros((micro, frames, width), jnp.float32)
    incoming = jnp.zeros((frames, width), jnp.bfloat16)
    ticks = micro + sections - 1
    for tick in range(ticks):
        slot = tick - (sections - 1 - rank)
        active = (slot >= 0) & (slot < micro)
        clipped = jnp.clip(slot, 0, micro - 1)
        dy = jnp.where(rank == sections - 1, top[clipped], incoming)
        dx, dz, dn, da = layer_backward(
            dy, masks[clipped], kernel, gain, proj, inv[clipped], nhat[clipped], slope[clipped]
        )
        dz_buf = dz_buf.at[clipped].set(jnp.where(active, dz, dz_buf[clipped]))
        dx_buf = dx_buf.at[clipped].set(jnp.where(active, dx, dx_buf[clipped]))
        dn_buf = dn_buf.at[clipped].set(jnp.where(active, dn, dn_buf[clipped]))
        da_buf = da_buf.at[clipped].set(jnp.where(active, da, da_buf[clipped]))
        if tick + 1 < ticks:
            incoming = from_behind(dx, "section", -1)

    h_all = h.reshape(rows, width)
    dz_all = dz_buf.reshape(rows, width)
    local = lax.dot_general(
        h_all, dz_all, (((0,), (0,)), ((), ())), preferred_element_type=jnp.float32
    )
    windows = jnp.stack([upad[:, j : j + frames] for j in range(taps)], axis=0)
    conv_acc = jnp.sum(windows * da_buf[None], axis=(1, 2))
    gain_acc = jnp.sum(dn_buf * nhat, axis=(0, 1))

    extra = jnp.concatenate([conv_acc.T, gain_acc[:, None]], axis=1)
    mine_p, mine_e = lax.psum_scatter((local, extra), "dp", scatter_dimension=0, tiled=True)
    mine = jnp.concatenate([mine_p, mine_e], axis=1)
    scale = 1.0 / groups
    proj_grad = mine[:, :width]
    conv_grad = mine[:, width : width + taps].T
    gain_grad = mine[:, width + taps]
    section_grads = dx_buf.reshape(rows, width)[None]
    return (
        section_grads,
        (proj_grad * scale)[None],
        (conv_grad * scale)[None],
        (gain_grad * scale)[None],
    )


def solution(mesh):
    return jax.shard_map(
        body,
        mesh=mesh,
        in_specs=(
            P("dp", None),
            P("section", "dp", None),
            P(),
            P("dp"),
            P("section", None, None),
            P("section", None),
            P("section", None, None),
        ),
        out_specs=(
            P("section", "dp", None),
            P("section", "dp", None),
            P("section", None, "dp"),
            P("section", "dp"),
        ),
        check_vma=False,
    )
```

```python
import jax
import jax.numpy as jnp
from jax import lax
from jax.sharding import PartitionSpec as P

eps = 1e-05


def from_behind(value, axis, by):
    size = lax.axis_size(axis)
    pairs = [(i, i + by) for i in range(size) if 0 <= i + by < size]
    return lax.ppermute(value, axis, pairs)


def sub_axes(groups):
    cores = 2
    along_z = 8
    along_x = groups // (cores * along_z)
    assert along_x * along_z * cores == groups
    return along_x, along_z, cores


def shifted(groups, stride, size, by):
    pairs = []
    for i in range(groups):
        pos = (i // stride) % size
        j = i + (((pos + by) % size) - pos) * stride
        pairs.append((i, j))
    return pairs


def ring_sum(chunks, axis, pos, size, pairs, by):
    def take(k):
        return lax.dynamic_index_in_dim(chunks, (pos - by * (1 + k)) % size, axis=axis, keepdims=False)

    send = take(0)
    for k in range(1, size):
        send = lax.ppermute(send, "dp", pairs) + take(k)
    return send


def reduce_scatter_dp(packed, groups):
    along_x, along_z, cores = sub_axes(groups)
    me = lax.axis_index("dp")
    core = me % cores
    zpos = (me // cores) % along_z
    xpos = me // (cores * along_z)
    rows, cols = packed.shape
    share = rows // groups
    blocks = packed.reshape(along_x, along_z, cores, share, cols)
    mixed = ring_sum(blocks, 2, core, cores, shifted(groups, 1, cores, 1), 1)
    half_z = along_z // 2
    up = ring_sum(mixed[:, :half_z], 0, xpos, along_x, shifted(groups, cores * along_z, along_x, 1), 1)
    down = ring_sum(mixed[:, half_z:], 0, xpos, along_x, shifted(groups, cores * along_z, along_x, -1), -1)
    by_z = jnp.concatenate([up, down], axis=0)
    half_c = cols // 2
    left = ring_sum(by_z[..., :half_c], 0, zpos, along_z, shifted(groups, cores, along_z, 1), 1)
    right = ring_sum(by_z[..., half_c:], 0, zpos, along_z, shifted(groups, cores, along_z, -1), -1)
    return jnp.concatenate([left, right], axis=1)


def layer_forward(x, mask, kernel):
    taps = kernel.shape[0]
    half = (taps - 1) // 2
    frames = x.shape[1]
    u = x.astype(jnp.float32) * mask
    upad = jnp.pad(u, ((0, 0), (half, half), (0, 0)))
    a = jnp.zeros(u.shape, jnp.float32)
    for j in range(taps):
        a = a + kernel[j] * upad[:, j : j + frames]
    return upad, a


def norm_forward(a, gain):
    mean = jnp.mean(a, axis=-1, keepdims=True)
    cen = a - mean
    var = jnp.mean(cen * cen, axis=-1, keepdims=True)
    inv = lax.rsqrt(var + eps)
    nhat = cen * inv
    n = nhat * gain
    sig = jax.nn.sigmoid(n)
    h = (n * sig).astype(jnp.bfloat16)
    slope = sig + n * sig * (1.0 - sig)
    return inv, nhat, h, slope


def layer_backward(dy, mask, kernel, gain, proj, inv, nhat, slope):
    taps = kernel.shape[0]
    half = (taps - 1) // 2
    frames = dy.shape[0]
    dz = (dy.astype(jnp.float32) * mask).astype(jnp.bfloat16)
    dh = lax.dot_general(dz, proj, (((1,), (1,)), ((), ())), preferred_element_type=jnp.float32)
    dn = dh * slope
    dnh = dn * gain
    da = inv * (
        dnh
        - jnp.mean(dnh, axis=-1, keepdims=True)
        - nhat * jnp.mean(dnh * nhat, axis=-1, keepdims=True)
    )
    dapad = jnp.pad(da, ((half, half), (0, 0)))
    du = jnp.zeros(da.shape, jnp.float32)
    for j in range(taps):
        du = du + kernel[j] * dapad[2 * half - j : 2 * half - j + frames]
    dx = (dy.astype(jnp.float32) + mask * du).astype(jnp.bfloat16)
    return dx, dz, dn, da


def body(grad_out, section_inputs, lengths, bucket_list, conv_weight, norm_gain, projection):
    sections = lax.axis_size("section")
    groups = lax.axis_size("dp")
    rank = lax.axis_index("section")
    micro = bucket_list.shape[0]
    rows, width = grad_out.shape
    frames = rows // micro
    table = jnp.arange(lengths.shape[0], dtype=jnp.int32)
    lens = jnp.sum(jnp.where(bucket_list[:, None] == table[None, :], lengths[None, :], 0), axis=1)
    masks = (jnp.arange(frames, dtype=jnp.int32)[None, :] < lens[:, None]).astype(jnp.float32)[
        ..., None
    ]
    saved = section_inputs[0].reshape(micro, frames, width)
    top = grad_out.reshape(micro, frames, width)
    kernel = conv_weight[0]
    gain = norm_gain[0]
    proj = projection[0]
    taps = kernel.shape[0]

    upad, a = layer_forward(saved, masks, kernel)
    inv, nhat, h, slope = norm_forward(a, gain)

    dz_buf = jnp.zeros((micro, frames, width), jnp.bfloat16)
    dx_buf = jnp.zeros((micro, frames, width), jnp.bfloat16)
    dn_buf = jnp.zeros((micro, frames, width), jnp.float32)
    da_buf = jnp.zeros((micro, frames, width), jnp.float32)
    incoming = jnp.zeros((frames, width), jnp.bfloat16)
    ticks = micro + sections - 1
    for tick in range(ticks):
        slot = tick - (sections - 1 - rank)
        active = (slot >= 0) & (slot < micro)
        clipped = jnp.clip(slot, 0, micro - 1)
        dy = jnp.where(rank == sections - 1, top[clipped], incoming)
        dx, dz, dn, da = layer_backward(
            dy, masks[clipped], kernel, gain, proj, inv[clipped], nhat[clipped], slope[clipped]
        )
        dz_buf = dz_buf.at[clipped].set(jnp.where(active, dz, dz_buf[clipped]))
        dx_buf = dx_buf.at[clipped].set(jnp.where(active, dx, dx_buf[clipped]))
        dn_buf = dn_buf.at[clipped].set(jnp.where(active, dn, dn_buf[clipped]))
        da_buf = da_buf.at[clipped].set(jnp.where(active, da, da_buf[clipped]))
        if tick + 1 < ticks:
            incoming = from_behind(dx, "section", -1)

    h_all = h.reshape(rows, width)
    dz_all = dz_buf.reshape(rows, width)
    local = lax.dot_general(
        h_all, dz_all, (((0,), (0,)), ((), ())), preferred_element_type=jnp.float32
    )
    windows = jnp.stack([upad[:, j : j + frames] for j in range(taps)], axis=0)
    conv_acc = jnp.sum(windows * da_buf[None], axis=(1, 2))
    gain_acc = jnp.sum(dn_buf * nhat, axis=(0, 1))

    packed = jnp.concatenate([local, conv_acc.T, gain_acc[:, None]], axis=1)
    mine = reduce_scatter_dp(packed, groups)
    scale = 1.0 / groups
    proj_grad = mine[:, :width]
    conv_grad = mine[:, width : width + taps].T
    gain_grad = mine[:, width + taps]
    section_grads = dx_buf.reshape(rows, width)[None]
    return (
        section_grads,
        (proj_grad * scale)[None],
        (conv_grad * scale)[None],
        (gain_grad * scale)[None],
    )


def solution(mesh):
    return jax.shard_map(
        body,
        mesh=mesh,
        in_specs=(
            P("dp", None),
            P("section", "dp", None),
            P(),
            P("dp"),
            P("section", None, None),
            P("section", None),
            P("section", None, None),
        ),
        out_specs=(
            P("section", "dp", None),
            P("section", "dp", None),
            P("section", None, "dp"),
            P("section", "dp"),
        ),
        check_vma=False,
    )
```

```python
import jax
import jax.numpy as jnp
from jax import lax
from jax.sharding import PartitionSpec as P

eps = 1e-05


def from_behind(value, axis, by):
    size = lax.axis_size(axis)
    pairs = [(i, i + by) for i in range(size) if 0 <= i + by < size]
    return lax.ppermute(value, axis, pairs)


def sub_axes(groups):
    cores = 2
    along_z = 8
    along_x = groups // (cores * along_z)
    assert along_x * along_z * cores == groups
    return along_x, along_z, cores


def shifted(groups, stride, size, by):
    pairs = []
    for i in range(groups):
        pos = (i // stride) % size
        j = i + (((pos + by) % size) - pos) * stride
        pairs.append((i, j))
    return pairs


def ring_sum(chunks, axis, pos, size, pairs, by):
    def take(k):
        return tuple(
            lax.dynamic_index_in_dim(c, (pos - by * (1 + k)) % size, axis=axis, keepdims=False)
            for c in chunks
        )

    send = take(0)
    for k in range(1, size):
        got = lax.ppermute(send, "dp", pairs)
        send = tuple(g + t for g, t in zip(got, take(k)))
    return send


def ring_meet(chunks, pos, size, groups, stride):
    ahead = size // 2
    behind = size - 1 - ahead

    def take(index):
        return tuple(
            lax.dynamic_index_in_dim(c, index % size, axis=0, keepdims=False) for c in chunks
        )

    total = take(pos)
    up = take(pos + ahead)
    down = take(pos - behind)
    up_pairs = shifted(groups, stride, size, 1)
    down_pairs = shifted(groups, stride, size, -1)
    for k in range(1, max(ahead, behind) + 1):
        if k <= ahead:
            got = lax.ppermute(up, "dp", up_pairs)
            up = tuple(g + t for g, t in zip(got, take(pos + ahead - k))) if k < ahead else got
        if k <= behind:
            got = lax.ppermute(down, "dp", down_pairs)
            down = tuple(g + t for g, t in zip(got, take(pos - behind + k))) if k < behind else got
    if ahead:
        total = tuple(a + b for a, b in zip(total, up))
    if behind:
        total = tuple(a + b for a, b in zip(total, down))
    return total


def reduce_scatter_dp(h_all, dz_all, extra, groups):
    along_x, along_z, cores = sub_axes(groups)
    me = lax.axis_index("dp")
    core = me % cores
    zpos = (me // cores) % along_z
    xpos = me // (cores * along_z)
    rows, width = h_all.shape
    share = width // groups

    def by_core(a, index, axis):
        parts = a.reshape(a.shape[:axis] + (along_x, along_z, cores, share) + a.shape[axis + 1 :])
        return lax.dynamic_index_in_dim(parts, index, axis=axis + 2, keepdims=False)

    def product(index):
        cols = by_core(h_all, index, 1).reshape(rows, width // cores)
        return lax.dot_general(cols, dz_all, (((0,), (0,)), ((), ())), preferred_element_type=jnp.float32)

    sent = (product(1 - core), by_core(extra, 1 - core, 0).reshape(width // cores, -1))
    got = lax.ppermute(sent, "dp", shifted(groups, 1, cores, 1))
    kept = (product(core), by_core(extra, core, 0).reshape(width // cores, -1))
    mixed = jnp.concatenate(
        [(g + k).reshape(along_x, along_z, share, -1) for g, k in zip(got, kept)], axis=-1
    )
    half_z = along_z // 2
    (up,) = ring_sum((mixed[:, :half_z],), 0, xpos, along_x,
                     shifted(groups, cores * along_z, along_x, 1), 1)
    (down,) = ring_sum((mixed[:, half_z:],), 0, xpos, along_x,
                       shifted(groups, cores * along_z, along_x, -1), -1)
    by_z = jnp.concatenate([up, down], axis=0)
    (mine,) = ring_meet((by_z,), zpos, along_z, groups, cores)
    return mine[:, :width], mine[:, width:]


def layer_forward(x, mask, kernel):
    taps = kernel.shape[0]
    half = (taps - 1) // 2
    frames = x.shape[1]
    u = x.astype(jnp.float32) * mask
    upad = jnp.pad(u, ((0, 0), (half, half), (0, 0)))
    a = jnp.zeros(u.shape, jnp.float32)
    for j in range(taps):
        a = a + kernel[j] * upad[:, j : j + frames]
    return upad, a


def norm_forward(a, gain):
    mean = jnp.mean(a, axis=-1, keepdims=True)
    cen = a - mean
    var = jnp.mean(cen * cen, axis=-1, keepdims=True)
    inv = lax.rsqrt(var + eps)
    nhat = cen * inv
    n = nhat * gain
    sig = jax.nn.sigmoid(n)
    h = (n * sig).astype(jnp.bfloat16)
    slope = sig + n * sig * (1.0 - sig)
    return inv, nhat, h, slope


def layer_backward(dy, mask, kernel, gain, proj, inv, nhat, slope):
    taps = kernel.shape[0]
    half = (taps - 1) // 2
    frames = dy.shape[0]
    dz = (dy.astype(jnp.float32) * mask).astype(jnp.bfloat16)
    dh = lax.dot_general(dz, proj, (((1,), (1,)), ((), ())), preferred_element_type=jnp.float32)
    dn = dh * slope
    dnh = dn * gain
    da = inv * (
        dnh
        - jnp.mean(dnh, axis=-1, keepdims=True)
        - nhat * jnp.mean(dnh * nhat, axis=-1, keepdims=True)
    )
    dapad = jnp.pad(da, ((half, half), (0, 0)))
    du = jnp.zeros(da.shape, jnp.float32)
    for j in range(taps):
        du = du + kernel[j] * dapad[2 * half - j : 2 * half - j + frames]
    dx = (dy.astype(jnp.float32) + mask * du).astype(jnp.bfloat16)
    return dx, dz, dn, da


def body(grad_out, section_inputs, lengths, bucket_list, conv_weight, norm_gain, projection):
    sections = lax.axis_size("section")
    groups = lax.axis_size("dp")
    rank = lax.axis_index("section")
    micro = bucket_list.shape[0]
    rows, width = grad_out.shape
    frames = rows // micro
    table = jnp.arange(lengths.shape[0], dtype=jnp.int32)
    lens = jnp.sum(jnp.where(bucket_list[:, None] == table[None, :], lengths[None, :], 0), axis=1)
    masks = (jnp.arange(frames, dtype=jnp.int32)[None, :] < lens[:, None]).astype(jnp.float32)[
        ..., None
    ]
    saved = section_inputs[0].reshape(micro, frames, width)
    top = grad_out.reshape(micro, frames, width)
    kernel = conv_weight[0]
    gain = norm_gain[0]
    proj = projection[0]
    taps = kernel.shape[0]

    upad, a = layer_forward(saved, masks, kernel)
    inv, nhat, h, slope = norm_forward(a, gain)

    dz_buf = jnp.zeros((micro, frames, width), jnp.bfloat16)
    dx_buf = jnp.zeros((micro, frames, width), jnp.bfloat16)
    conv_acc = jnp.zeros(kernel.shape, jnp.float32)
    gain_acc = jnp.zeros((width,), jnp.float32)
    incoming = jnp.zeros((frames, width), jnp.bfloat16)
    ticks = micro + sections - 1
    for tick in range(ticks):
        slot = tick - (sections - 1 - rank)
        active = (slot >= 0) & (slot < micro)
        clipped = jnp.clip(slot, 0, micro - 1)
        dy = jnp.where(rank == sections - 1, top[clipped], incoming)
        dx, dz, dn, da = layer_backward(
            dy, masks[clipped], kernel, gain, proj, inv[clipped], nhat[clipped], slope[clipped]
        )
        if tick + 1 < ticks:
            incoming = from_behind(dx, "section", -1)
        dz_buf = dz_buf.at[clipped].set(jnp.where(active, dz, dz_buf[clipped]))
        dx_buf = dx_buf.at[clipped].set(jnp.where(active, dx, dx_buf[clipped]))
        held = upad[clipped]
        windows = jnp.stack([held[j : j + frames] for j in range(taps)], axis=0)
        conv_acc = conv_acc + jnp.where(active, jnp.sum(windows * da[None], axis=1), 0.0)
        gain_acc = gain_acc + jnp.where(active, jnp.sum(dn * nhat[clipped], axis=0), 0.0)

    extra = jnp.concatenate([conv_acc.T, gain_acc[:, None]], axis=1)
    mine, mine_extra = reduce_scatter_dp(
        h.reshape(rows, width), dz_buf.reshape(rows, width), extra, groups
    )
    scale = 1.0 / groups
    proj_grad = mine.reshape(-1, width)
    mine_extra = mine_extra.reshape(-1, taps + 1)
    conv_grad = mine_extra[:, :taps].T
    gain_grad = mine_extra[:, taps]
    section_grads = dx_buf.reshape(rows, width)[None]
    return (
        section_grads,
        (proj_grad * scale)[None],
        (conv_grad * scale)[None],
        (gain_grad * scale)[None],
    )


def solution(mesh):
    return jax.shard_map(
        body,
        mesh=mesh,
        in_specs=(
            P("dp", None),
            P("section", "dp", None),
            P(),
            P("dp"),
            P("section", None, None),
            P("section", None),
            P("section", None, None),
        ),
        out_specs=(
            P("section", "dp", None),
            P("section", "dp", None),
            P("section", None, "dp"),
            P("section", "dp"),
        ),
        check_vma=False,
    )
```

```python
import jax
import jax.numpy as jnp
from jax import lax
from jax.experimental import pallas as pl
from jax.experimental.pallas import tpu as pltpu
from jax.sharding import PartitionSpec as P

eps = 1e-05


def from_behind(value, axis, by):
    size = lax.axis_size(axis)
    pairs = [(i, i + by) for i in range(size) if 0 <= i + by < size]
    return lax.ppermute(value, axis, pairs)


def sub_axes(groups):
    cores = 2
    along_z = 8
    along_x = groups // (cores * along_z)
    assert along_x * along_z * cores == groups
    return along_x, along_z, cores


def shifted(groups, stride, size, by):
    pairs = []
    for i in range(groups):
        pos = (i // stride) % size
        j = i + (((pos + by) % size) - pos) * stride
        pairs.append((i, j))
    return pairs


def ring_sum(chunks, axis, pos, size, pairs, by):
    def take(k):
        return tuple(
            lax.dynamic_index_in_dim(c, (pos - by * (1 + k)) % size, axis=axis, keepdims=False)
            for c in chunks
        )

    send = take(0)
    for k in range(1, size):
        got = lax.ppermute(send, "dp", pairs)
        send = tuple(g + t for g, t in zip(got, take(k)))
    return send


def ring_meet(chunks, pos, size, groups, stride):
    ahead = size // 2
    behind = size - 1 - ahead

    def take(index):
        return tuple(
            lax.dynamic_index_in_dim(c, index % size, axis=0, keepdims=False) for c in chunks
        )

    total = take(pos)
    up = take(pos + ahead)
    down = take(pos - behind)
    up_pairs = shifted(groups, stride, size, 1)
    down_pairs = shifted(groups, stride, size, -1)
    for k in range(1, max(ahead, behind) + 1):
        if k <= ahead:
            got = lax.ppermute(up, "dp", up_pairs)
            up = tuple(g + t for g, t in zip(got, take(pos + ahead - k))) if k < ahead else got
        if k <= behind:
            got = lax.ppermute(down, "dp", down_pairs)
            down = tuple(g + t for g, t in zip(got, take(pos - behind + k))) if k < behind else got
    if ahead:
        total = tuple(a + b for a, b in zip(total, up))
    if behind:
        total = tuple(a + b for a, b in zip(total, down))
    return total


def reduce_scatter_dp(h_all, dz_all, extra, groups):
    along_x, along_z, cores = sub_axes(groups)
    me = lax.axis_index("dp")
    core = me % cores
    zpos = (me // cores) % along_z
    xpos = me // (cores * along_z)
    rows, width = h_all.shape
    share = width // groups

    def by_core(a, index, axis):
        parts = a.reshape(a.shape[:axis] + (along_x, along_z, cores, share) + a.shape[axis + 1 :])
        return lax.dynamic_index_in_dim(parts, index, axis=axis + 2, keepdims=False)

    def product(index):
        cols = by_core(h_all, index, 1).reshape(rows, width // cores)
        return lax.dot_general(cols, dz_all, (((0,), (0,)), ((), ())), preferred_element_type=jnp.float32)

    sent = (product(1 - core), by_core(extra, 1 - core, 0).reshape(width // cores, -1))
    got = lax.ppermute(sent, "dp", shifted(groups, 1, cores, 1))
    kept = (product(core), by_core(extra, core, 0).reshape(width // cores, -1))
    mixed = jnp.concatenate(
        [(g + k).reshape(along_x, along_z, share, -1) for g, k in zip(got, kept)], axis=-1
    )
    half_z = along_z // 2
    (up,) = ring_sum((mixed[:, :half_z],), 0, xpos, along_x,
                     shifted(groups, cores * along_z, along_x, 1), 1)
    (down,) = ring_sum((mixed[:, half_z:],), 0, xpos, along_x,
                       shifted(groups, cores * along_z, along_x, -1), -1)
    by_z = jnp.concatenate([up, down], axis=0)
    (mine,) = ring_meet((by_z,), zpos, along_z, groups, cores)
    return mine[:, :width], mine[:, width:]


def conv_grad_kernel(u_ref, da_ref, out_ref):
    frames = da_ref.shape[0]

    def tap(j, carry):
        acc = jnp.zeros(out_ref.shape[1:], jnp.float32)
        for t in range(frames):
            acc = acc + da_ref[t] * u_ref[j + t]
        out_ref[j] = acc
        return carry

    lax.fori_loop(0, out_ref.shape[0], tap, 0)


def window_products(u_t, da_t, taps):
    frames = da_t.shape[0]
    shape = (taps,) + da_t.shape[1:]
    size = da_t.size
    return pl.pallas_call(
        conv_grad_kernel,
        out_shape=jax.ShapeDtypeStruct(shape, jnp.float32),
        in_specs=[pl.BlockSpec(memory_space=pltpu.VMEM)] * 2,
        out_specs=pl.BlockSpec(memory_space=pltpu.VMEM),
        cost_estimate=pl.CostEstimate(
            flops=2 * taps * size, transcendentals=0, bytes_accessed=4 * (u_t.size + size + taps * size // frames)
        ),
    )(u_t, da_t)


def layer_forward(x, mask, kernel):
    taps = kernel.shape[0]
    half = (taps - 1) // 2
    frames = x.shape[1]
    u = x.astype(jnp.float32) * mask
    upad = jnp.pad(u, ((0, 0), (half, half), (0, 0)))
    a = jnp.zeros(u.shape, jnp.float32)
    for j in range(taps):
        a = a + kernel[j] * upad[:, j : j + frames]
    return upad, a


def norm_forward(a, gain):
    mean = jnp.mean(a, axis=-1, keepdims=True)
    cen = a - mean
    var = jnp.mean(cen * cen, axis=-1, keepdims=True)
    inv = lax.rsqrt(var + eps)
    nhat = cen * inv
    n = nhat * gain
    sig = jax.nn.sigmoid(n)
    h = (n * sig).astype(jnp.bfloat16)
    slope = sig + n * sig * (1.0 - sig)
    return inv, nhat, h, slope


def layer_backward(dy, mask, kernel, gain, proj, inv, nhat, slope):
    taps = kernel.shape[0]
    half = (taps - 1) // 2
    frames = dy.shape[0]
    dz = (dy.astype(jnp.float32) * mask).astype(jnp.bfloat16)
    dh = lax.dot_general(dz, proj, (((1,), (1,)), ((), ())), preferred_element_type=jnp.float32)
    dn = dh * slope
    dnh = dn * gain
    da = inv * (
        dnh
        - jnp.mean(dnh, axis=-1, keepdims=True)
        - nhat * jnp.mean(dnh * nhat, axis=-1, keepdims=True)
    )
    dapad = jnp.pad(da, ((half, half), (0, 0)))
    du = jnp.zeros(da.shape, jnp.float32)
    for j in range(taps):
        du = du + kernel[j] * dapad[2 * half - j : 2 * half - j + frames]
    dx = (dy.astype(jnp.float32) + mask * du).astype(jnp.bfloat16)
    return dx, dz, dn, da


def body(grad_out, section_inputs, lengths, bucket_list, conv_weight, norm_gain, projection):
    sections = lax.axis_size("section")
    groups = lax.axis_size("dp")
    rank = lax.axis_index("section")
    micro = bucket_list.shape[0]
    rows, width = grad_out.shape
    frames = rows // micro
    table = jnp.arange(lengths.shape[0], dtype=jnp.int32)
    lens = jnp.sum(jnp.where(bucket_list[:, None] == table[None, :], lengths[None, :], 0), axis=1)
    masks = (jnp.arange(frames, dtype=jnp.int32)[None, :] < lens[:, None]).astype(jnp.float32)[
        ..., None
    ]
    saved = section_inputs[0].reshape(micro, frames, width)
    top = grad_out.reshape(micro, frames, width)
    kernel = conv_weight[0]
    gain = norm_gain[0]
    proj = projection[0]
    taps = kernel.shape[0]

    upad, a = layer_forward(saved, masks, kernel)
    inv, nhat, h, slope = norm_forward(a, gain)

    dz_buf = jnp.zeros((micro, frames, width), jnp.bfloat16)
    dx_buf = jnp.zeros((micro, frames, width), jnp.bfloat16)
    dn_buf = jnp.zeros((micro, frames, width), jnp.float32)
    da_buf = jnp.zeros((micro, frames, width), jnp.float32)
    incoming = jnp.zeros((frames, width), jnp.bfloat16)
    ticks = micro + sections - 1
    for tick in range(ticks):
        slot = tick - (sections - 1 - rank)
        active = (slot >= 0) & (slot < micro)
        clipped = jnp.clip(slot, 0, micro - 1)
        dy = jnp.where(rank == sections - 1, top[clipped], incoming)
        dx, dz, dn, da = layer_backward(
            dy, masks[clipped], kernel, gain, proj, inv[clipped], nhat[clipped], slope[clipped]
        )
        if tick + 1 < ticks:
            incoming = from_behind(dx, "section", -1)
        dz_buf = dz_buf.at[clipped].set(jnp.where(active, dz, dz_buf[clipped]))
        dx_buf = dx_buf.at[clipped].set(jnp.where(active, dx, dx_buf[clipped]))
        dn_buf = dn_buf.at[clipped].set(jnp.where(active, dn, dn_buf[clipped]))
        da_buf = da_buf.at[clipped].set(jnp.where(active, da, da_buf[clipped]))

    half = (taps - 1) // 2
    lanes = width * micro // 8
    u_t = jnp.pad(upad[:, half : half + frames].transpose(1, 0, 2), ((half, half), (0, 0), (0, 0)))
    u_t = u_t.reshape(frames + 2 * half, 8, lanes)
    da_t = da_buf.transpose(1, 0, 2).reshape(frames, 8, lanes)
    conv_acc = window_products(u_t, da_t, taps).reshape(taps, micro, width).sum(axis=1)
    gain_acc = jnp.sum(dn_buf * nhat, axis=(0, 1))

    extra = jnp.concatenate([conv_acc.T, gain_acc[:, None]], axis=1)
    mine, mine_extra = reduce_scatter_dp(
        h.reshape(rows, width), dz_buf.reshape(rows, width), extra, groups
    )
    scale = 1.0 / groups
    proj_grad = mine.reshape(-1, width)
    mine_extra = mine_extra.reshape(-1, taps + 1)
    conv_grad = mine_extra[:, :taps].T
    gain_grad = mine_extra[:, taps]
    section_grads = dx_buf.reshape(rows, width)[None]
    return (
        section_grads,
        (proj_grad * scale)[None],
        (conv_grad * scale)[None],
        (gain_grad * scale)[None],
    )


def solution(mesh):
    return jax.shard_map(
        body,
        mesh=mesh,
        in_specs=(
            P("dp", None),
            P("section", "dp", None),
            P(),
            P("dp"),
            P("section", None, None),
            P("section", None),
            P("section", None, None),
        ),
        out_specs=(
            P("section", "dp", None),
            P("section", "dp", None),
            P("section", None, "dp"),
            P("section", "dp"),
        ),
        check_vma=False,
    )
```

```python
import jax
import jax.numpy as jnp
from jax import lax
from jax.experimental import pallas as pl
from jax.experimental.pallas import tpu as pltpu
from jax.sharding import PartitionSpec as P

eps = 1e-05


def from_behind(value, axis, by):
    size = lax.axis_size(axis)
    pairs = [(i, i + by) for i in range(size) if 0 <= i + by < size]
    return lax.ppermute(value, axis, pairs)


def sub_axes(groups):
    cores = 2
    along_z = 8
    along_x = groups // (cores * along_z)
    assert along_x * along_z * cores == groups
    return along_x, along_z, cores


def shifted(groups, stride, size, by):
    pairs = []
    for i in range(groups):
        pos = (i // stride) % size
        j = i + (((pos + by) % size) - pos) * stride
        pairs.append((i, j))
    return pairs


def ring_sum(chunks, axis, pos, size, pairs, by):
    def take(k):
        return tuple(
            lax.dynamic_index_in_dim(c, (pos - by * (1 + k)) % size, axis=axis, keepdims=False)
            for c in chunks
        )

    send = take(0)
    for k in range(1, size):
        got = lax.ppermute(send, "dp", pairs)
        send = tuple(g + t for g, t in zip(got, take(k)))
    return send


def ring_meet(chunks, pos, size, groups, stride):
    ahead = size // 2
    behind = size - 1 - ahead

    def take(index):
        return tuple(
            lax.dynamic_index_in_dim(c, index % size, axis=0, keepdims=False) for c in chunks
        )

    total = take(pos)
    up = take(pos + ahead)
    down = take(pos - behind)
    up_pairs = shifted(groups, stride, size, 1)
    down_pairs = shifted(groups, stride, size, -1)
    for k in range(1, max(ahead, behind) + 1):
        if k <= ahead:
            got = lax.ppermute(up, "dp", up_pairs)
            up = tuple(g + t for g, t in zip(got, take(pos + ahead - k))) if k < ahead else got
        if k <= behind:
            got = lax.ppermute(down, "dp", down_pairs)
            down = tuple(g + t for g, t in zip(got, take(pos - behind + k))) if k < behind else got
    if ahead:
        total = tuple(a + b for a, b in zip(total, up))
    if behind:
        total = tuple(a + b for a, b in zip(total, down))
    return total


def reduce_scatter_dp(h_all, dz_all, extra_of, groups):
    along_x, along_z, cores = sub_axes(groups)
    me = lax.axis_index("dp")
    core = me % cores
    zpos = (me // cores) % along_z
    xpos = me // (cores * along_z)
    rows, width = h_all.shape
    share = width // groups

    def by_core(a, index, axis):
        parts = a.reshape(a.shape[:axis] + (along_x, along_z, cores, share) + a.shape[axis + 1 :])
        return lax.dynamic_index_in_dim(parts, index, axis=axis + 2, keepdims=False)

    def product(index):
        cols = by_core(h_all, index, 1).reshape(rows, width // cores)
        return lax.dot_general(cols, dz_all, (((0,), (0,)), ((), ())), preferred_element_type=jnp.float32)

    sent = product(1 - core)
    got = lax.ppermute(sent, "dp", shifted(groups, 1, cores, 1))
    extra = extra_of(sent)
    got = (got, lax.ppermute(by_core(extra, 1 - core, 0).reshape(width // cores, -1), "dp",
                             shifted(groups, 1, cores, 1)))
    kept = (product(core), by_core(extra, core, 0).reshape(width // cores, -1))
    mixed = jnp.concatenate(
        [(g + k).reshape(along_x, along_z, share, -1) for g, k in zip(got, kept)], axis=-1
    )
    half_z = along_z // 2
    (up,) = ring_sum((mixed[:, :half_z],), 0, xpos, along_x,
                     shifted(groups, cores * along_z, along_x, 1), 1)
    (down,) = ring_sum((mixed[:, half_z:],), 0, xpos, along_x,
                       shifted(groups, cores * along_z, along_x, -1), -1)
    by_z = jnp.concatenate([up, down], axis=0)
    (mine,) = ring_meet((by_z,), zpos, along_z, groups, cores)
    return mine[:, :width], mine[:, width:]


def conv_grad_kernel(u_ref, da_ref, out_ref):
    frames = da_ref.shape[0]

    def tap(j, carry):
        acc = jnp.zeros(out_ref.shape[1:], jnp.float32)
        for t in range(frames):
            acc = acc + da_ref[t] * u_ref[j + t]
        out_ref[j] = acc
        return carry

    lax.fori_loop(0, out_ref.shape[0], tap, 0)


def window_products(u_t, da_t, taps):
    frames = da_t.shape[0]
    shape = (taps,) + da_t.shape[1:]
    size = da_t.size
    return pl.pallas_call(
        conv_grad_kernel,
        out_shape=jax.ShapeDtypeStruct(shape, jnp.float32),
        in_specs=[pl.BlockSpec(memory_space=pltpu.VMEM)] * 2,
        out_specs=pl.BlockSpec(memory_space=pltpu.VMEM),
        cost_estimate=pl.CostEstimate(
            flops=2 * taps * size, transcendentals=0, bytes_accessed=4 * (u_t.size + size + taps * size // frames)
        ),
    )(u_t, da_t)


def layer_forward(x, mask, kernel):
    taps = kernel.shape[0]
    half = (taps - 1) // 2
    frames = x.shape[1]
    u = x.astype(jnp.float32) * mask
    upad = jnp.pad(u, ((0, 0), (half, half), (0, 0)))
    a = jnp.zeros(u.shape, jnp.float32)
    for j in range(taps):
        a = a + kernel[j] * upad[:, j : j + frames]
    return upad, a


def norm_forward(a, gain):
    mean = jnp.mean(a, axis=-1, keepdims=True)
    cen = a - mean
    var = jnp.mean(cen * cen, axis=-1, keepdims=True)
    inv = lax.rsqrt(var + eps)
    nhat = cen * inv
    n = nhat * gain
    sig = jax.nn.sigmoid(n)
    h = (n * sig).astype(jnp.bfloat16)
    slope = sig + n * sig * (1.0 - sig)
    return inv, nhat, h, slope


def layer_backward(dy, mask, kernel, gain, proj, inv, nhat, slope):
    taps = kernel.shape[0]
    half = (taps - 1) // 2
    frames = dy.shape[0]
    dz = (dy.astype(jnp.float32) * mask).astype(jnp.bfloat16)
    dh = lax.dot_general(dz, proj, (((1,), (1,)), ((), ())), preferred_element_type=jnp.float32)
    dn = dh * slope
    dnh = dn * gain
    da = inv * (
        dnh
        - jnp.mean(dnh, axis=-1, keepdims=True)
        - nhat * jnp.mean(dnh * nhat, axis=-1, keepdims=True)
    )
    dapad = jnp.pad(da, ((half, half), (0, 0)))
    du = jnp.zeros(da.shape, jnp.float32)
    for j in range(taps):
        du = du + kernel[j] * dapad[2 * half - j : 2 * half - j + frames]
    dx = (dy.astype(jnp.float32) + mask * du).astype(jnp.bfloat16)
    return dx, dz, dn, da


def body(grad_out, section_inputs, lengths, bucket_list, conv_weight, norm_gain, projection):
    sections = lax.axis_size("section")
    groups = lax.axis_size("dp")
    rank = lax.axis_index("section")
    micro = bucket_list.shape[0]
    rows, width = grad_out.shape
    frames = rows // micro
    table = jnp.arange(lengths.shape[0], dtype=jnp.int32)
    lens = jnp.sum(jnp.where(bucket_list[:, None] == table[None, :], lengths[None, :], 0), axis=1)
    masks = (jnp.arange(frames, dtype=jnp.int32)[None, :] < lens[:, None]).astype(jnp.float32)[
        ..., None
    ]
    saved = section_inputs[0].reshape(micro, frames, width)
    top = grad_out.reshape(micro, frames, width)
    kernel = conv_weight[0]
    gain = norm_gain[0]
    proj = projection[0]
    taps = kernel.shape[0]

    upad, a = layer_forward(saved, masks, kernel)
    inv, nhat, h, slope = norm_forward(a, gain)

    dz_buf = jnp.zeros((micro, frames, width), jnp.bfloat16)
    dx_buf = jnp.zeros((micro, frames, width), jnp.bfloat16)
    dn_buf = jnp.zeros((micro, frames, width), jnp.float32)
    da_buf = jnp.zeros((micro, frames, width), jnp.float32)
    incoming = jnp.zeros((frames, width), jnp.bfloat16)
    ticks = micro + sections - 1
    for tick in range(ticks):
        slot = tick - (sections - 1 - rank)
        active = (slot >= 0) & (slot < micro)
        clipped = jnp.clip(slot, 0, micro - 1)
        dy = jnp.where(rank == sections - 1, top[clipped], incoming)
        dx, dz, dn, da = layer_backward(
            dy, masks[clipped], kernel, gain, proj, inv[clipped], nhat[clipped], slope[clipped]
        )
        if tick + 1 < ticks:
            incoming = from_behind(dx, "section", -1)
        dz_buf = dz_buf.at[clipped].set(jnp.where(active, dz, dz_buf[clipped]))
        dx_buf = dx_buf.at[clipped].set(jnp.where(active, dx, dx_buf[clipped]))
        dn_buf = dn_buf.at[clipped].set(jnp.where(active, dn, dn_buf[clipped]))
        da_buf = da_buf.at[clipped].set(jnp.where(active, da, da_buf[clipped]))

    def extra_of(after):
        held, da_all, dn_all, nhat_all, _ = lax.optimization_barrier((upad, da_buf, dn_buf, nhat, after))
        half = (taps - 1) // 2
        lanes = width * micro // 8
        u_t = jnp.pad(held[:, half : half + frames].transpose(1, 0, 2), ((half, half), (0, 0), (0, 0)))
        u_t = u_t.reshape(frames + 2 * half, 8, lanes)
        da_t = da_all.transpose(1, 0, 2).reshape(frames, 8, lanes)
        conv_acc = window_products(u_t, da_t, taps).reshape(taps, micro, width).sum(axis=1)
        gain_acc = jnp.sum(dn_all * nhat_all, axis=(0, 1))
        return jnp.concatenate([conv_acc.T, gain_acc[:, None]], axis=1)

    h_late, dz_all = lax.optimization_barrier((h, dz_buf))
    mine, mine_extra = reduce_scatter_dp(
        h_late.reshape(rows, width), dz_all.reshape(rows, width), extra_of, groups
    )
    scale = 1.0 / groups
    proj_grad = mine.reshape(-1, width)
    mine_extra = mine_extra.reshape(-1, taps + 1)
    conv_grad = mine_extra[:, :taps].T
    gain_grad = mine_extra[:, taps]
    section_grads = dx_buf.reshape(rows, width)[None]
    return (
        section_grads,
        (proj_grad * scale)[None],
        (conv_grad * scale)[None],
        (gain_grad * scale)[None],
    )


def solution(mesh):
    return jax.shard_map(
        body,
        mesh=mesh,
        in_specs=(
            P("dp", None),
            P("section", "dp", None),
            P(),
            P("dp"),
            P("section", None, None),
            P("section", None),
            P("section", None, None),
        ),
        out_specs=(
            P("section", "dp", None),
            P("section", "dp", None),
            P("section", None, "dp"),
            P("section", "dp"),
        ),
        check_vma=False,
    )
```

```python
import jax
import jax.numpy as jnp
from jax import lax
from jax.experimental import pallas as pl
from jax.experimental.pallas import tpu as pltpu
from jax.sharding import PartitionSpec as P

eps = 1e-05


def from_behind(value, axis, by):
    size = lax.axis_size(axis)
    pairs = [(i, i + by) for i in range(size) if 0 <= i + by < size]
    return lax.ppermute(value, axis, pairs)


def sub_axes(groups):
    cores = 2
    along_z = 8
    along_x = groups // (cores * along_z)
    assert along_x * along_z * cores == groups
    return along_x, along_z, cores


def shifted(groups, stride, size, by):
    pairs = []
    for i in range(groups):
        pos = (i // stride) % size
        j = i + (((pos + by) % size) - pos) * stride
        pairs.append((i, j))
    return pairs


def ring_sum(chunks, axis, pos, size, pairs, by):
    def take(k):
        return tuple(
            lax.dynamic_index_in_dim(c, (pos - by * (1 + k)) % size, axis=axis, keepdims=False)
            for c in chunks
        )

    send = take(0)
    for k in range(1, size):
        got = lax.ppermute(send, "dp", pairs)
        send = tuple(g + t for g, t in zip(got, take(k)))
    return send


def ring_meet(chunks, pos, size, groups, stride, axis=0):
    ahead = size // 2
    behind = size - 1 - ahead

    def take(index):
        return tuple(
            lax.dynamic_index_in_dim(c, index % size, axis=axis, keepdims=False) for c in chunks
        )

    total = take(pos)
    up = take(pos + ahead)
    down = take(pos - behind)
    up_pairs = shifted(groups, stride, size, 1)
    down_pairs = shifted(groups, stride, size, -1)
    for k in range(1, max(ahead, behind) + 1):
        if k <= ahead:
            got = lax.ppermute(up, "dp", up_pairs)
            up = tuple(g + t for g, t in zip(got, take(pos + ahead - k))) if k < ahead else got
        if k <= behind:
            got = lax.ppermute(down, "dp", down_pairs)
            down = tuple(g + t for g, t in zip(got, take(pos - behind + k))) if k < behind else got
    if ahead:
        total = tuple(a + b for a, b in zip(total, up))
    if behind:
        total = tuple(a + b for a, b in zip(total, down))
    return total


def reduce_scatter_dp(h_all, dz_all, extra, groups):
    along_x, along_z, cores = sub_axes(groups)
    me = lax.axis_index("dp")
    core = me % cores
    zpos = (me // cores) % along_z
    xpos = me // (cores * along_z)
    rows, width = h_all.shape
    share = width // groups

    def by_core(a, index, axis):
        parts = a.reshape(a.shape[:axis] + (along_x, along_z, cores, share) + a.shape[axis + 1 :])
        return lax.dynamic_index_in_dim(parts, index, axis=axis + 2, keepdims=False)

    def product(index):
        cols = by_core(h_all, index, 1).reshape(rows, width // cores)
        return lax.dot_general(cols, dz_all, (((0,), (0,)), ((), ())), preferred_element_type=jnp.float32)

    sent = (product(1 - core), by_core(extra, 1 - core, 0).reshape(width // cores, -1))
    got = lax.ppermute(sent, "dp", shifted(groups, 1, cores, 1))
    kept = (product(core), by_core(extra, core, 0).reshape(width // cores, -1))
    mixed = jnp.concatenate(
        [(g + k).reshape(along_x, along_z, share, -1) for g, k in zip(got, kept)], axis=-1
    )
    x_pairs = (shifted(groups, cores * along_z, along_x, 1), shifted(groups, cores * along_z, along_x, -1))
    split = mixed.shape[-1] // 2
    first, second = mixed[..., :split], mixed[..., split:]
    half_z = along_z // 2
    (up,) = ring_sum((first[:, :half_z],), 0, xpos, along_x, x_pairs[0], 1)
    (down,) = ring_sum((first[:, half_z:],), 0, xpos, along_x, x_pairs[1], -1)
    (second_z,) = ring_meet((second,), zpos, along_z, groups, cores, axis=1)
    (first_xz,) = ring_meet((jnp.concatenate([up, down], axis=0),), zpos, along_z, groups, cores)
    quarter = second_z.shape[-1] // 2
    (left,) = ring_sum((second_z[..., :quarter],), 0, xpos, along_x, x_pairs[0], 1)
    (right,) = ring_sum((second_z[..., quarter:],), 0, xpos, along_x, x_pairs[1], -1)
    mine = jnp.concatenate([first_xz, left, right], axis=-1)
    return mine[:, :width], mine[:, width:]


def conv_grad_kernel(u_ref, da_ref, out_ref):
    frames = da_ref.shape[0]

    def tap(j, carry):
        acc = jnp.zeros(out_ref.shape[1:], jnp.float32)
        for t in range(frames):
            acc = acc + da_ref[t] * u_ref[j + t]
        out_ref[j] = acc
        return carry

    lax.fori_loop(0, out_ref.shape[0], tap, 0)


def window_products(u_t, da_t, taps):
    frames = da_t.shape[0]
    shape = (taps,) + da_t.shape[1:]
    size = da_t.size
    return pl.pallas_call(
        conv_grad_kernel,
        out_shape=jax.ShapeDtypeStruct(shape, jnp.float32),
        in_specs=[pl.BlockSpec(memory_space=pltpu.VMEM)] * 2,
        out_specs=pl.BlockSpec(memory_space=pltpu.VMEM),
        cost_estimate=pl.CostEstimate(
            flops=2 * taps * size, transcendentals=0, bytes_accessed=4 * (u_t.size + size + taps * size // frames)
        ),
    )(u_t, da_t)


def layer_forward(x, mask, kernel):
    taps = kernel.shape[0]
    half = (taps - 1) // 2
    frames = x.shape[1]
    u = x.astype(jnp.float32) * mask
    upad = jnp.pad(u, ((0, 0), (half, half), (0, 0)))
    a = jnp.zeros(u.shape, jnp.float32)
    for j in range(taps):
        a = a + kernel[j] * upad[:, j : j + frames]
    return upad, a


def norm_forward(a, gain):
    mean = jnp.mean(a, axis=-1, keepdims=True)
    cen = a - mean
    var = jnp.mean(cen * cen, axis=-1, keepdims=True)
    inv = lax.rsqrt(var + eps)
    nhat = cen * inv
    n = nhat * gain
    sig = jax.nn.sigmoid(n)
    h = (n * sig).astype(jnp.bfloat16)
    slope = sig + n * sig * (1.0 - sig)
    return inv, nhat, h, slope


def layer_backward(dy, mask, kernel, gain, proj, inv, nhat, slope):
    taps = kernel.shape[0]
    half = (taps - 1) // 2
    frames = dy.shape[0]
    dz = (dy.astype(jnp.float32) * mask).astype(jnp.bfloat16)
    dh = lax.dot_general(dz, proj, (((1,), (1,)), ((), ())), preferred_element_type=jnp.float32)
    dn = dh * slope
    dnh = dn * gain
    da = inv * (
        dnh
        - jnp.mean(dnh, axis=-1, keepdims=True)
        - nhat * jnp.mean(dnh * nhat, axis=-1, keepdims=True)
    )
    dapad = jnp.pad(da, ((half, half), (0, 0)))
    du = jnp.zeros(da.shape, jnp.float32)
    for j in range(taps):
        du = du + kernel[j] * dapad[2 * half - j : 2 * half - j + frames]
    dx = (dy.astype(jnp.float32) + mask * du).astype(jnp.bfloat16)
    return dx, dz, dn, da


def body(grad_out, section_inputs, lengths, bucket_list, conv_weight, norm_gain, projection):
    sections = lax.axis_size("section")
    groups = lax.axis_size("dp")
    rank = lax.axis_index("section")
    micro = bucket_list.shape[0]
    rows, width = grad_out.shape
    frames = rows // micro
    table = jnp.arange(lengths.shape[0], dtype=jnp.int32)
    lens = jnp.sum(jnp.where(bucket_list[:, None] == table[None, :], lengths[None, :], 0), axis=1)
    masks = (jnp.arange(frames, dtype=jnp.int32)[None, :] < lens[:, None]).astype(jnp.float32)[
        ..., None
    ]
    saved = section_inputs[0].reshape(micro, frames, width)
    top = grad_out.reshape(micro, frames, width)
    kernel = conv_weight[0]
    gain = norm_gain[0]
    proj = projection[0]
    taps = kernel.shape[0]

    upad, a = layer_forward(saved, masks, kernel)
    inv, nhat, h, slope = norm_forward(a, gain)

    dz_buf = jnp.zeros((micro, frames, width), jnp.bfloat16)
    dx_buf = jnp.zeros((micro, frames, width), jnp.bfloat16)
    dn_buf = jnp.zeros((micro, frames, width), jnp.float32)
    da_buf = jnp.zeros((micro, frames, width), jnp.float32)
    incoming = jnp.zeros((frames, width), jnp.bfloat16)
    ticks = micro + sections - 1
    for tick in range(ticks):
        slot = tick - (sections - 1 - rank)
        active = (slot >= 0) & (slot < micro)
        clipped = jnp.clip(slot, 0, micro - 1)
        dy = jnp.where(rank == sections - 1, top[clipped], incoming)
        dx, dz, dn, da = layer_backward(
            dy, masks[clipped], kernel, gain, proj, inv[clipped], nhat[clipped], slope[clipped]
        )
        if tick + 1 < ticks:
            incoming = from_behind(dx, "section", -1)
        dz_buf = dz_buf.at[clipped].set(jnp.where(active, dz, dz_buf[clipped]))
        dx_buf = dx_buf.at[clipped].set(jnp.where(active, dx, dx_buf[clipped]))
        dn_buf = dn_buf.at[clipped].set(jnp.where(active, dn, dn_buf[clipped]))
        da_buf = da_buf.at[clipped].set(jnp.where(active, da, da_buf[clipped]))

    half = (taps - 1) // 2
    lanes = width * micro // 8
    u_t = jnp.pad(upad[:, half : half + frames].transpose(1, 0, 2), ((half, half), (0, 0), (0, 0)))
    u_t = u_t.reshape(frames + 2 * half, 8, lanes)
    da_t = da_buf.transpose(1, 0, 2).reshape(frames, 8, lanes)
    conv_acc = window_products(u_t, da_t, taps).reshape(taps, micro, width).sum(axis=1)
    gain_acc = jnp.sum(dn_buf * nhat, axis=(0, 1))

    extra = jnp.concatenate([conv_acc.T, gain_acc[:, None]], axis=1)
    mine, mine_extra = reduce_scatter_dp(
        h.reshape(rows, width), dz_buf.reshape(rows, width), extra, groups
    )
    scale = 1.0 / groups
    proj_grad = mine.reshape(-1, width)
    mine_extra = mine_extra.reshape(-1, taps + 1)
    conv_grad = mine_extra[:, :taps].T
    gain_grad = mine_extra[:, taps]
    section_grads = dx_buf.reshape(rows, width)[None]
    return (
        section_grads,
        (proj_grad * scale)[None],
        (conv_grad * scale)[None],
        (gain_grad * scale)[None],
    )


def solution(mesh):
    return jax.shard_map(
        body,
        mesh=mesh,
        in_specs=(
            P("dp", None),
            P("section", "dp", None),
            P(),
            P("dp"),
            P("section", None, None),
            P("section", None),
            P("section", None, None),
        ),
        out_specs=(
            P("section", "dp", None),
            P("section", "dp", None),
            P("section", None, "dp"),
            P("section", "dp"),
        ),
        check_vma=False,
    )
```

```python
import jax
import jax.numpy as jnp
from jax import lax
from jax.experimental import pallas as pl
from jax.experimental.pallas import tpu as pltpu
from jax.sharding import PartitionSpec as P

eps = 1e-05


def from_behind(value, axis, by):
    size = lax.axis_size(axis)
    pairs = [(i, i + by) for i in range(size) if 0 <= i + by < size]
    return lax.ppermute(value, axis, pairs)


def sub_axes(groups):
    cores = 2
    along_z = 8
    along_x = groups // (cores * along_z)
    assert along_x * along_z * cores == groups
    return along_x, along_z, cores


def shifted(groups, stride, size, by):
    pairs = []
    for i in range(groups):
        pos = (i // stride) % size
        j = i + (((pos + by) % size) - pos) * stride
        pairs.append((i, j))
    return pairs


def ring_sum(chunks, axis, pos, size, pairs, by):
    def take(k):
        return tuple(
            lax.dynamic_index_in_dim(c, (pos - by * (1 + k)) % size, axis=axis, keepdims=False)
            for c in chunks
        )

    send = take(0)
    for k in range(1, size):
        got = lax.ppermute(send, "dp", pairs)
        send = tuple(g + t for g, t in zip(got, take(k)))
    return send


def ring_meet(chunks, pos, size, groups, stride):
    ahead = size // 2
    behind = size - 1 - ahead

    def take(index):
        return tuple(
            lax.dynamic_index_in_dim(c, index % size, axis=0, keepdims=False) for c in chunks
        )

    total = take(pos)
    up = take(pos + ahead)
    down = take(pos - behind)
    up_pairs = shifted(groups, stride, size, 1)
    down_pairs = shifted(groups, stride, size, -1)
    for k in range(1, max(ahead, behind) + 1):
        if k <= ahead:
            got = lax.ppermute(up, "dp", up_pairs)
            up = tuple(g + t for g, t in zip(got, take(pos + ahead - k))) if k < ahead else got
        if k <= behind:
            got = lax.ppermute(down, "dp", down_pairs)
            down = tuple(g + t for g, t in zip(got, take(pos - behind + k))) if k < behind else got
    if ahead:
        total = tuple(a + b for a, b in zip(total, up))
    if behind:
        total = tuple(a + b for a, b in zip(total, down))
    return total


def reduce_scatter_dp(h_all, dz_all, extra, groups):
    along_x, along_z, cores = sub_axes(groups)
    me = lax.axis_index("dp")
    core = me % cores
    zpos = (me // cores) % along_z
    xpos = me // (cores * along_z)
    rows, width = h_all.shape
    share = width // groups

    def by_core(a, index, axis):
        parts = a.reshape(a.shape[:axis] + (along_x, along_z, cores, share) + a.shape[axis + 1 :])
        return lax.dynamic_index_in_dim(parts, index, axis=axis + 2, keepdims=False)

    def product(index):
        cols = by_core(h_all, index, 1).reshape(rows, width // cores)
        return lax.dot_general(cols, dz_all, (((0,), (0,)), ((), ())), preferred_element_type=jnp.float32)

    sent = (product(1 - core), by_core(extra, 1 - core, 0).reshape(width // cores, -1))
    got = lax.ppermute(sent, "dp", shifted(groups, 1, cores, 1))
    kept = (product(core), by_core(extra, core, 0).reshape(width // cores, -1))
    mixed = jnp.concatenate(
        [(g + k).reshape(along_x, along_z, share, -1) for g, k in zip(got, kept)], axis=-1
    )
    half_z = along_z // 2
    (up,) = ring_sum((mixed[:, :half_z],), 0, xpos, along_x,
                     shifted(groups, cores * along_z, along_x, 1), 1)
    (down,) = ring_sum((mixed[:, half_z:],), 0, xpos, along_x,
                       shifted(groups, cores * along_z, along_x, -1), -1)
    by_z = jnp.concatenate([up, down], axis=0)
    (mine,) = ring_meet((by_z,), zpos, along_z, groups, cores)
    return mine[:, :width], mine[:, width:]


def conv_grad_kernel(u_ref, da_ref, out_ref):
    micro, frames, width = da_ref.shape
    for j in range(out_ref.shape[0]):
        acc = jnp.zeros((8, width), jnp.float32)
        for m in range(micro):
            prod = da_ref[m] * u_ref[m, j : j + frames, :]
            acc = acc + prod.reshape(frames // 8, 8, width).sum(axis=0)
        out_ref[j : j + 1, :] = acc.sum(axis=0, keepdims=True)


def window_products(upad, da, taps):
    micro, frames, width = da.shape
    return pl.pallas_call(
        conv_grad_kernel,
        out_shape=jax.ShapeDtypeStruct((taps, width), jnp.float32),
        in_specs=[pl.BlockSpec(memory_space=pltpu.VMEM)] * 2,
        out_specs=pl.BlockSpec(memory_space=pltpu.VMEM),
        cost_estimate=pl.CostEstimate(
            flops=2 * taps * da.size, transcendentals=0, bytes_accessed=4 * (upad.size + da.size + taps * width)
        ),
    )(upad, da)


def layer_forward(x, mask, kernel):
    taps = kernel.shape[0]
    half = (taps - 1) // 2
    frames = x.shape[1]
    u = x.astype(jnp.float32) * mask
    upad = jnp.pad(u, ((0, 0), (half, half), (0, 0)))
    a = jnp.zeros(u.shape, jnp.float32)
    for j in range(taps):
        a = a + kernel[j] * upad[:, j : j + frames]
    return upad, a


def norm_forward(a, gain):
    mean = jnp.mean(a, axis=-1, keepdims=True)
    cen = a - mean
    var = jnp.mean(cen * cen, axis=-1, keepdims=True)
    inv = lax.rsqrt(var + eps)
    nhat = cen * inv
    n = nhat * gain
    sig = jax.nn.sigmoid(n)
    h = (n * sig).astype(jnp.bfloat16)
    slope = sig + n * sig * (1.0 - sig)
    return inv, nhat, h, slope


def layer_backward(dy, mask, kernel, gain, proj, inv, nhat, slope):
    taps = kernel.shape[0]
    half = (taps - 1) // 2
    frames = dy.shape[0]
    dz = (dy.astype(jnp.float32) * mask).astype(jnp.bfloat16)
    dh = lax.dot_general(dz, proj, (((1,), (1,)), ((), ())), preferred_element_type=jnp.float32)
    dn = dh * slope
    dnh = dn * gain
    da = inv * (
        dnh
        - jnp.mean(dnh, axis=-1, keepdims=True)
        - nhat * jnp.mean(dnh * nhat, axis=-1, keepdims=True)
    )
    dapad = jnp.pad(da, ((half, half), (0, 0)))
    du = jnp.zeros(da.shape, jnp.float32)
    for j in range(taps):
        du = du + kernel[j] * dapad[2 * half - j : 2 * half - j + frames]
    dx = (dy.astype(jnp.float32) + mask * du).astype(jnp.bfloat16)
    return dx, dz, dn, da


def body(grad_out, section_inputs, lengths, bucket_list, conv_weight, norm_gain, projection):
    sections = lax.axis_size("section")
    groups = lax.axis_size("dp")
    rank = lax.axis_index("section")
    micro = bucket_list.shape[0]
    rows, width = grad_out.shape
    frames = rows // micro
    table = jnp.arange(lengths.shape[0], dtype=jnp.int32)
    lens = jnp.sum(jnp.where(bucket_list[:, None] == table[None, :], lengths[None, :], 0), axis=1)
    masks = (jnp.arange(frames, dtype=jnp.int32)[None, :] < lens[:, None]).astype(jnp.float32)[
        ..., None
    ]
    saved = section_inputs[0].reshape(micro, frames, width)
    top = grad_out.reshape(micro, frames, width)
    kernel = conv_weight[0]
    gain = norm_gain[0]
    proj = projection[0]
    taps = kernel.shape[0]

    upad, a = layer_forward(saved, masks, kernel)
    inv, nhat, h, slope = norm_forward(a, gain)

    dz_buf = jnp.zeros((micro, frames, width), jnp.bfloat16)
    dx_buf = jnp.zeros((micro, frames, width), jnp.bfloat16)
    dn_buf = jnp.zeros((micro, frames, width), jnp.float32)
    da_buf = jnp.zeros((micro, frames, width), jnp.float32)
    incoming = jnp.zeros((frames, width), jnp.bfloat16)
    ticks = micro + sections - 1
    for tick in range(ticks):
        slot = tick - (sections - 1 - rank)
        active = (slot >= 0) & (slot < micro)
        clipped = jnp.clip(slot, 0, micro - 1)
        dy = jnp.where(rank == sections - 1, top[clipped], incoming)
        dx, dz, dn, da = layer_backward(
            dy, masks[clipped], kernel, gain, proj, inv[clipped], nhat[clipped], slope[clipped]
        )
        if tick + 1 < ticks:
            incoming = from_behind(dx, "section", -1)
        dz_buf = dz_buf.at[clipped].set(jnp.where(active, dz, dz_buf[clipped]))
        dx_buf = dx_buf.at[clipped].set(jnp.where(active, dx, dx_buf[clipped]))
        dn_buf = dn_buf.at[clipped].set(jnp.where(active, dn, dn_buf[clipped]))
        da_buf = da_buf.at[clipped].set(jnp.where(active, da, da_buf[clipped]))

    conv_acc = window_products(upad, da_buf, taps)
    gain_acc = jnp.sum(dn_buf * nhat, axis=(0, 1))

    extra = jnp.concatenate([conv_acc.T, gain_acc[:, None]], axis=1)
    mine, mine_extra = reduce_scatter_dp(
        h.reshape(rows, width), dz_buf.reshape(rows, width), extra, groups
    )
    scale = 1.0 / groups
    proj_grad = mine.reshape(-1, width)
    mine_extra = mine_extra.reshape(-1, taps + 1)
    conv_grad = mine_extra[:, :taps].T
    gain_grad = mine_extra[:, taps]
    section_grads = dx_buf.reshape(rows, width)[None]
    return (
        section_grads,
        (proj_grad * scale)[None],
        (conv_grad * scale)[None],
        (gain_grad * scale)[None],
    )


def solution(mesh):
    return jax.shard_map(
        body,
        mesh=mesh,
        in_specs=(
            P("dp", None),
            P("section", "dp", None),
            P(),
            P("dp"),
            P("section", None, None),
            P("section", None),
            P("section", None, None),
        ),
        out_specs=(
            P("section", "dp", None),
            P("section", "dp", None),
            P("section", None, "dp"),
            P("section", "dp"),
        ),
        check_vma=False,
    )
```

```python
import jax
import jax.numpy as jnp
from jax import lax
from jax.experimental import pallas as pl
from jax.experimental.pallas import tpu as pltpu
from jax.sharding import PartitionSpec as P

eps = 1e-05


def from_behind(value, axis, by):
    size = lax.axis_size(axis)
    pairs = [(i, i + by) for i in range(size) if 0 <= i + by < size]
    return lax.ppermute(value, axis, pairs)


def sub_axes(groups):
    cores = 2
    along_z = 8
    along_x = groups // (cores * along_z)
    assert along_x * along_z * cores == groups
    return along_x, along_z, cores


def shifted(groups, stride, size, by):
    pairs = []
    for i in range(groups):
        pos = (i // stride) % size
        j = i + (((pos + by) % size) - pos) * stride
        pairs.append((i, j))
    return pairs


def ring_sum(chunks, axis, pos, size, pairs, by):
    def take(k):
        return tuple(
            lax.dynamic_index_in_dim(c, (pos - by * (1 + k)) % size, axis=axis, keepdims=False)
            for c in chunks
        )

    send = take(0)
    for k in range(1, size):
        got = lax.ppermute(send, "dp", pairs)
        send = tuple(g + t for g, t in zip(got, take(k)))
    return send


def ring_meet(chunks, pos, size, groups, stride):
    ahead = size // 2
    behind = size - 1 - ahead

    def take(index):
        return tuple(
            lax.dynamic_index_in_dim(c, index % size, axis=0, keepdims=False) for c in chunks
        )

    total = take(pos)
    up = take(pos + ahead)
    down = take(pos - behind)
    up_pairs = shifted(groups, stride, size, 1)
    down_pairs = shifted(groups, stride, size, -1)
    for k in range(1, max(ahead, behind) + 1):
        if k <= ahead:
            got = lax.ppermute(up, "dp", up_pairs)
            up = tuple(g + t for g, t in zip(got, take(pos + ahead - k))) if k < ahead else got
        if k <= behind:
            got = lax.ppermute(down, "dp", down_pairs)
            down = tuple(g + t for g, t in zip(got, take(pos - behind + k))) if k < behind else got
    if ahead:
        total = tuple(a + b for a, b in zip(total, up))
    if behind:
        total = tuple(a + b for a, b in zip(total, down))
    return total


def reduce_scatter_dp(h_all, dz_all, extra, groups):
    along_x, along_z, cores = sub_axes(groups)
    me = lax.axis_index("dp")
    core = me % cores
    zpos = (me // cores) % along_z
    xpos = me // (cores * along_z)
    rows, width = h_all.shape
    share = width // groups

    def by_core(a, index, axis):
        parts = a.reshape(a.shape[:axis] + (along_x, along_z, cores, share) + a.shape[axis + 1 :])
        return lax.dynamic_index_in_dim(parts, index, axis=axis + 2, keepdims=False)

    def product(index):
        cols = by_core(h_all, index, 1).reshape(rows, width // cores)
        return lax.dot_general(cols, dz_all, (((0,), (0,)), ((), ())), preferred_element_type=jnp.float32)

    sent = (product(1 - core), by_core(extra, 1 - core, 0).reshape(width // cores, -1))
    got = lax.ppermute(sent, "dp", shifted(groups, 1, cores, 1))
    kept = (product(core), by_core(extra, core, 0).reshape(width // cores, -1))
    mixed = jnp.concatenate(
        [(g + k).reshape(along_x, along_z, share, -1) for g, k in zip(got, kept)], axis=-1
    )
    half_z = along_z // 2
    (up,) = ring_sum((mixed[:, :half_z],), 0, xpos, along_x,
                     shifted(groups, cores * along_z, along_x, 1), 1)
    (down,) = ring_sum((mixed[:, half_z:],), 0, xpos, along_x,
                       shifted(groups, cores * along_z, along_x, -1), -1)
    by_z = jnp.concatenate([up, down], axis=0)
    (mine,) = ring_meet((by_z,), zpos, along_z, groups, cores)
    return mine[:, :width], mine[:, width:]


def conv_grad_kernel(u_ref, da_ref, out_ref):
    micro, frames, width = da_ref.shape
    for j in range(out_ref.shape[0]):
        acc = jnp.zeros((8, width), jnp.float32)
        for m in range(micro):
            prod = da_ref[m] * u_ref[m, j : j + frames, :]
            acc = acc + prod.reshape(frames // 8, 8, width).sum(axis=0)
        out_ref[j : j + 1, :] = acc.sum(axis=0, keepdims=True)


def window_products(upad, da, taps):
    micro, frames, width = da.shape
    return pl.pallas_call(
        conv_grad_kernel,
        out_shape=jax.ShapeDtypeStruct((taps, width), jnp.float32),
        in_specs=[pl.BlockSpec(memory_space=pltpu.VMEM)] * 2,
        out_specs=pl.BlockSpec(memory_space=pltpu.VMEM),
        cost_estimate=pl.CostEstimate(
            flops=2 * taps * da.size, transcendentals=0, bytes_accessed=4 * (upad.size + da.size + taps * width)
        ),
    )(upad, da)


def layer_forward(x, mask, kernel):
    taps = kernel.shape[0]
    half = (taps - 1) // 2
    frames = x.shape[1]
    u = x.astype(jnp.float32) * mask
    upad = jnp.pad(u, ((0, 0), (half, half), (0, 0)))
    a = jnp.zeros(u.shape, jnp.float32)
    for j in range(taps):
        a = a + kernel[j] * upad[:, j : j + frames]
    return upad, a


def norm_forward(a, gain):
    mean = jnp.mean(a, axis=-1, keepdims=True)
    cen = a - mean
    var = jnp.mean(cen * cen, axis=-1, keepdims=True)
    inv = lax.rsqrt(var + eps)
    nhat = cen * inv
    n = nhat * gain
    sig = jax.nn.sigmoid(n)
    h = (n * sig).astype(jnp.bfloat16)
    slope = sig + n * sig * (1.0 - sig)
    return inv, nhat, h, slope


def layer_backward(dy, mask, kernel, gain, proj, inv, nhat, slope):
    taps = kernel.shape[0]
    half = (taps - 1) // 2
    frames = dy.shape[0]
    dz = (dy.astype(jnp.float32) * mask).astype(jnp.bfloat16)
    dh = lax.dot_general(dz, proj, (((1,), (1,)), ((), ())), preferred_element_type=jnp.float32)
    dn = dh * slope
    dnh = dn * gain
    da = inv * (
        dnh
        - jnp.mean(dnh, axis=-1, keepdims=True)
        - nhat * jnp.mean(dnh * nhat, axis=-1, keepdims=True)
    )
    dapad = jnp.pad(da, ((half, half), (0, 0)))
    du = jnp.zeros(da.shape, jnp.float32)
    for j in range(taps):
        du = du + kernel[j] * dapad[2 * half - j : 2 * half - j + frames]
    dx = (dy.astype(jnp.float32) + mask * du).astype(jnp.bfloat16)
    return dx, dz, dn, da


def body(grad_out, section_inputs, lengths, bucket_list, conv_weight, norm_gain, projection):
    sections = lax.axis_size("section")
    groups = lax.axis_size("dp")
    rank = lax.axis_index("section")
    micro = bucket_list.shape[0]
    rows, width = grad_out.shape
    frames = rows // micro
    table = jnp.arange(lengths.shape[0], dtype=jnp.int32)
    lens = jnp.sum(jnp.where(bucket_list[:, None] == table[None, :], lengths[None, :], 0), axis=1)
    masks = (jnp.arange(frames, dtype=jnp.int32)[None, :] < lens[:, None]).astype(jnp.float32)[
        ..., None
    ]
    saved = section_inputs[0].reshape(micro, frames, width)
    top = grad_out.reshape(micro, frames, width)
    kernel = conv_weight[0]
    gain = norm_gain[0]
    proj = projection[0]
    taps = kernel.shape[0]

    upad, a = layer_forward(saved, masks, kernel)
    inv, nhat, h, slope = norm_forward(a, gain)

    dz_buf = jnp.zeros((micro, frames, width), jnp.bfloat16)
    dx_buf = jnp.zeros((micro, frames, width), jnp.bfloat16)
    dn_buf = jnp.zeros((micro, frames, width), jnp.float32)
    da_buf = jnp.zeros((micro, frames, width), jnp.float32)
    incoming = jnp.zeros((frames, width), jnp.bfloat16)
    ticks = micro + sections - 1
    for tick in range(ticks):
        slot = tick - (sections - 1 - rank)
        active = (slot >= 0) & (slot < micro)
        clipped = jnp.clip(slot, 0, micro - 1)
        dy = jnp.where(rank == sections - 1, top[clipped], incoming)
        dx, dz, dn, da = layer_backward(
            dy, masks[clipped], kernel, gain, proj, inv[clipped], nhat[clipped], slope[clipped]
        )
        if tick == ticks // 2:
            h, dx = lax.optimization_barrier((h, dx))
        if tick + 1 < ticks:
            incoming = from_behind(dx, "section", -1)
        dz_buf = dz_buf.at[clipped].set(jnp.where(active, dz, dz_buf[clipped]))
        dx_buf = dx_buf.at[clipped].set(jnp.where(active, dx, dx_buf[clipped]))
        dn_buf = dn_buf.at[clipped].set(jnp.where(active, dn, dn_buf[clipped]))
        da_buf = da_buf.at[clipped].set(jnp.where(active, da, da_buf[clipped]))

    conv_acc = window_products(upad, da_buf, taps)
    gain_acc = jnp.sum(dn_buf * nhat, axis=(0, 1))

    extra = jnp.concatenate([conv_acc.T, gain_acc[:, None]], axis=1)
    mine, mine_extra = reduce_scatter_dp(
        h.reshape(rows, width), dz_buf.reshape(rows, width), extra, groups
    )
    scale = 1.0 / groups
    proj_grad = mine.reshape(-1, width)
    mine_extra = mine_extra.reshape(-1, taps + 1)
    conv_grad = mine_extra[:, :taps].T
    gain_grad = mine_extra[:, taps]
    section_grads = dx_buf.reshape(rows, width)[None]
    return (
        section_grads,
        (proj_grad * scale)[None],
        (conv_grad * scale)[None],
        (gain_grad * scale)[None],
    )


def solution(mesh):
    return jax.shard_map(
        body,
        mesh=mesh,
        in_specs=(
            P("dp", None),
            P("section", "dp", None),
            P(),
            P("dp"),
            P("section", None, None),
            P("section", None),
            P("section", None, None),
        ),
        out_specs=(
            P("section", "dp", None),
            P("section", "dp", None),
            P("section", None, "dp"),
            P("section", "dp"),
        ),
        check_vma=False,
    )
```

```python
import jax
import jax.numpy as jnp
from jax import lax
from jax.experimental import pallas as pl
from jax.experimental.pallas import tpu as pltpu
from jax.sharding import PartitionSpec as P

eps = 1e-05


def from_behind(value, axis, by):
    size = lax.axis_size(axis)
    pairs = [(i, i + by) for i in range(size) if 0 <= i + by < size]
    return lax.ppermute(value, axis, pairs)


def sub_axes(groups):
    cores = 2
    along_z = 8
    along_x = groups // (cores * along_z)
    assert along_x * along_z * cores == groups
    return along_x, along_z, cores


def shifted(groups, stride, size, by):
    pairs = []
    for i in range(groups):
        pos = (i // stride) % size
        j = i + (((pos + by) % size) - pos) * stride
        pairs.append((i, j))
    return pairs


def ring_sum(chunks, axis, pos, size, pairs, by):
    def take(k):
        return tuple(
            lax.dynamic_index_in_dim(c, (pos - by * (1 + k)) % size, axis=axis, keepdims=False)
            for c in chunks
        )

    send = take(0)
    for k in range(1, size):
        got = lax.ppermute(send, "dp", pairs)
        send = tuple(g + t for g, t in zip(got, take(k)))
    return send


def ring_meet(chunks, pos, size, groups, stride):
    ahead = size // 2
    behind = size - 1 - ahead

    def take(index):
        return tuple(
            lax.dynamic_index_in_dim(c, index % size, axis=0, keepdims=False) for c in chunks
        )

    total = take(pos)
    up = take(pos + ahead)
    down = take(pos - behind)
    up_pairs = shifted(groups, stride, size, 1)
    down_pairs = shifted(groups, stride, size, -1)
    for k in range(1, max(ahead, behind) + 1):
        if k <= ahead:
            got = lax.ppermute(up, "dp", up_pairs)
            up = tuple(g + t for g, t in zip(got, take(pos + ahead - k))) if k < ahead else got
        if k <= behind:
            got = lax.ppermute(down, "dp", down_pairs)
            down = tuple(g + t for g, t in zip(got, take(pos - behind + k))) if k < behind else got
    if ahead:
        total = tuple(a + b for a, b in zip(total, up))
    if behind:
        total = tuple(a + b for a, b in zip(total, down))
    return total


def reduce_scatter_dp(h_all, dz_all, extra, groups):
    along_x, along_z, cores = sub_axes(groups)
    me = lax.axis_index("dp")
    core = me % cores
    zpos = (me // cores) % along_z
    xpos = me // (cores * along_z)
    rows, width = h_all.shape
    share = width // groups

    def by_core(a, index, axis):
        parts = a.reshape(a.shape[:axis] + (along_x, along_z, cores, share) + a.shape[axis + 1 :])
        return lax.dynamic_index_in_dim(parts, index, axis=axis + 2, keepdims=False)

    def product(index):
        cols = by_core(h_all, index, 1).reshape(rows, width // cores)
        return lax.dot_general(cols, dz_all, (((0,), (0,)), ((), ())), preferred_element_type=jnp.float32)

    sent = (product(1 - core), by_core(extra, 1 - core, 0).reshape(width // cores, -1))
    got = lax.ppermute(sent, "dp", shifted(groups, 1, cores, 1))
    kept = (product(core), by_core(extra, core, 0).reshape(width // cores, -1))
    mixed = jnp.concatenate(
        [(g + k).reshape(along_x, along_z, share, -1) for g, k in zip(got, kept)], axis=-1
    )
    half_z = along_z // 2
    (up,) = ring_sum((mixed[:, :half_z],), 0, xpos, along_x,
                     shifted(groups, cores * along_z, along_x, 1), 1)
    (down,) = ring_sum((mixed[:, half_z:],), 0, xpos, along_x,
                       shifted(groups, cores * along_z, along_x, -1), -1)
    by_z = jnp.concatenate([up, down], axis=0)
    (mine,) = ring_meet((by_z,), zpos, along_z, groups, cores)
    return mine[:, :width], mine[:, width:]


def conv_grad_kernel(u_ref, da_ref, dn_ref, nhat_ref, out_ref):
    micro, frames, width = da_ref.shape
    taps = out_ref.shape[0] - 1
    for j in range(taps):
        acc = jnp.zeros((8, width), jnp.float32)
        for m in range(micro):
            prod = da_ref[m] * u_ref[m, j : j + frames, :]
            acc = acc + prod.reshape(frames // 8, 8, width).sum(axis=0)
        out_ref[j : j + 1, :] = acc.sum(axis=0, keepdims=True)
    acc = jnp.zeros((8, width), jnp.float32)
    for m in range(micro):
        prod = dn_ref[m] * nhat_ref[m]
        acc = acc + prod.reshape(frames // 8, 8, width).sum(axis=0)
    out_ref[taps : taps + 1, :] = acc.sum(axis=0, keepdims=True)


def window_products(upad, da, dn, nhat, taps):
    micro, frames, width = da.shape
    return pl.pallas_call(
        conv_grad_kernel,
        out_shape=jax.ShapeDtypeStruct((taps + 1, width), jnp.float32),
        in_specs=[pl.BlockSpec(memory_space=pltpu.VMEM)] * 4,
        out_specs=pl.BlockSpec(memory_space=pltpu.VMEM),
        cost_estimate=pl.CostEstimate(
            flops=2 * (taps + 1) * da.size, transcendentals=0,
            bytes_accessed=4 * (upad.size + 3 * da.size + (taps + 1) * width),
        ),
    )(upad, da, dn, nhat)


def layer_forward(x, mask, kernel):
    taps = kernel.shape[0]
    half = (taps - 1) // 2
    frames = x.shape[1]
    u = x.astype(jnp.float32) * mask
    upad = jnp.pad(u, ((0, 0), (half, half), (0, 0)))
    a = jnp.zeros(u.shape, jnp.float32)
    for j in range(taps):
        a = a + kernel[j] * upad[:, j : j + frames]
    return upad, a


def norm_forward(a, gain):
    mean = jnp.mean(a, axis=-1, keepdims=True)
    cen = a - mean
    var = jnp.mean(cen * cen, axis=-1, keepdims=True)
    inv = lax.rsqrt(var + eps)
    nhat = cen * inv
    n = nhat * gain
    sig = jax.nn.sigmoid(n)
    h = (n * sig).astype(jnp.bfloat16)
    slope = sig + n * sig * (1.0 - sig)
    return inv, nhat, h, slope


def layer_backward(dy, mask, kernel, gain, proj, inv, nhat, slope):
    taps = kernel.shape[0]
    half = (taps - 1) // 2
    frames = dy.shape[0]
    dz = (dy.astype(jnp.float32) * mask).astype(jnp.bfloat16)
    dh = lax.dot_general(dz, proj, (((1,), (1,)), ((), ())), preferred_element_type=jnp.float32)
    dn = dh * slope
    dnh = dn * gain
    da = inv * (
        dnh
        - jnp.mean(dnh, axis=-1, keepdims=True)
        - nhat * jnp.mean(dnh * nhat, axis=-1, keepdims=True)
    )
    dapad = jnp.pad(da, ((half, half), (0, 0)))
    du = jnp.zeros(da.shape, jnp.float32)
    for j in range(taps):
        du = du + kernel[j] * dapad[2 * half - j : 2 * half - j + frames]
    dx = (dy.astype(jnp.float32) + mask * du).astype(jnp.bfloat16)
    return dx, dz, dn, da


def body(grad_out, section_inputs, lengths, bucket_list, conv_weight, norm_gain, projection):
    sections = lax.axis_size("section")
    groups = lax.axis_size("dp")
    rank = lax.axis_index("section")
    micro = bucket_list.shape[0]
    rows, width = grad_out.shape
    frames = rows // micro
    table = jnp.arange(lengths.shape[0], dtype=jnp.int32)
    lens = jnp.sum(jnp.where(bucket_list[:, None] == table[None, :], lengths[None, :], 0), axis=1)
    masks = (jnp.arange(frames, dtype=jnp.int32)[None, :] < lens[:, None]).astype(jnp.float32)[
        ..., None
    ]
    saved = section_inputs[0].reshape(micro, frames, width)
    top = grad_out.reshape(micro, frames, width)
    kernel = conv_weight[0]
    gain = norm_gain[0]
    proj = projection[0]
    taps = kernel.shape[0]

    upad, a = layer_forward(saved, masks, kernel)
    inv, nhat, h, slope = norm_forward(a, gain)

    dz_buf = jnp.zeros((micro, frames, width), jnp.bfloat16)
    dx_buf = jnp.zeros((micro, frames, width), jnp.bfloat16)
    dn_buf = jnp.zeros((micro, frames, width), jnp.float32)
    da_buf = jnp.zeros((micro, frames, width), jnp.float32)
    incoming = jnp.zeros((frames, width), jnp.bfloat16)
    ticks = micro + sections - 1
    for tick in range(ticks):
        slot = tick - (sections - 1 - rank)
        active = (slot >= 0) & (slot < micro)
        clipped = jnp.clip(slot, 0, micro - 1)
        dy = jnp.where(rank == sections - 1, top[clipped], incoming)
        dx, dz, dn, da = layer_backward(
            dy, masks[clipped], kernel, gain, proj, inv[clipped], nhat[clipped], slope[clipped]
        )
        if tick + 1 < ticks:
            incoming = from_behind(dx, "section", -1)
        dz_buf = dz_buf.at[clipped].set(jnp.where(active, dz, dz_buf[clipped]))
        dx_buf = dx_buf.at[clipped].set(jnp.where(active, dx, dx_buf[clipped]))
        dn_buf = dn_buf.at[clipped].set(jnp.where(active, dn, dn_buf[clipped]))
        da_buf = da_buf.at[clipped].set(jnp.where(active, da, da_buf[clipped]))

    extra = window_products(upad, da_buf, dn_buf, nhat, taps).T
    mine, mine_extra = reduce_scatter_dp(
        h.reshape(rows, width), dz_buf.reshape(rows, width), extra, groups
    )
    scale = 1.0 / groups
    proj_grad = mine.reshape(-1, width)
    mine_extra = mine_extra.reshape(-1, taps + 1)
    conv_grad = mine_extra[:, :taps].T
    gain_grad = mine_extra[:, taps]
    section_grads = dx_buf.reshape(rows, width)[None]
    return (
        section_grads,
        (proj_grad * scale)[None],
        (conv_grad * scale)[None],
        (gain_grad * scale)[None],
    )


def solution(mesh):
    return jax.shard_map(
        body,
        mesh=mesh,
        in_specs=(
            P("dp", None),
            P("section", "dp", None),
            P(),
            P("dp"),
            P("section", None, None),
            P("section", None),
            P("section", None, None),
        ),
        out_specs=(
            P("section", "dp", None),
            P("section", "dp", None),
            P("section", None, "dp"),
            P("section", "dp"),
        ),
        check_vma=False,
    )
```
